1024 devices in a mesh: dom: 32 (over z, core), grp: 8 (over y), rep: 4 (over x).
Axes of the slice: x: 4, y: 8, z: 16, core: 2. Of those that a mesh axis runs over, the one named last changes fastest.
Arguments:
- features: bfloat16 [8192, 768], P(('rep', 'grp')), may hold values from -6 to 6
- tiles: bfloat16 [32, 4, 12, 256, 256], P('dom', 'rep', None, 'grp'), may hold values from 0 to 0.039794922
- columns: int32 [2, 32, 4, 8], replicated, may hold values from 0 to 7, as said below
- counts: int32 [2, 32, 4], replicated, may hold values from 1 to 8, as said below
- weights: bfloat16 [2, 768, 768], replicated, may hold values from -0.21875 to 0.21875
Outputs:
- aggregated: bfloat16 [8192, 768], P(('dom', 'grp', 'rep'))
The draws below stay inside these ranges and needn't reach their ends.
Inputs may be any that keep to these rules, and one draw needn't show every extreme that they name: `columns`: within each list, the entries below the count name distinct source panels of the group; later entries are unused. An owner's two counts in a column group add up to 9 to 15, and 15 is reached; over all owners of a column group they add up to 384.
All inputs are finite; a program needn't handle non-finite values.
Results may differ from the reference program's by a relative error of at most 0.0085.
Values may be sent and summed in bfloat16 or wider, within the bound.
No kernel may reach another device: no remote copies, remote signals or barrier semaphores. Data moves between devices by JAX's collectives and lax.ppermute only.
A program may use at most 32 MiB of HBM per device.

```python
import jax
import jax.numpy as jnp
from jax import lax

FEAT = 768
TILE = 256
LMAX = 8
WORK = 12
SRC = 8192
N_DOM = 32
N_GRP = 8
N_REP = 4


def plan_lists(key):
    base = jax.random.fold_in(key, 4242)
    keys = jax.random.split(base, 5)
    half_owners = N_DOM // 2
    spread = jax.random.randint(keys[0], (N_REP, half_owners), LMAX + 1, 2 * LMAX)
    spread = spread.at[:, 0].set(LMAX + 1)
    paired = jnp.stack([3 * LMAX - spread, spread], axis=2).reshape(N_REP, N_DOM)
    shuffles = jax.vmap(lambda sub: jax.random.permutation(sub, N_DOM))(jax.random.split(keys[1], N_REP))
    group_rows = jnp.arange(N_REP, dtype=jnp.int32)[:, None] * jnp.ones((1, N_DOM), jnp.int32)
    loads = jnp.zeros((N_REP, N_DOM), jnp.int32).at[group_rows, shuffles].set(paired)
    upper = jnp.minimum(loads, LMAX)
    lower = jnp.maximum(loads - LMAX, 0)
    draw_bits = jax.random.randint(keys[2], (N_REP, N_DOM), 0, 1 << 20)
    first_count = lower + draw_bits % (upper - lower + 1)
    first_count = jnp.where(loads == 2 * LMAX - 1, upper, first_count)
    swapped = jax.random.randint(keys[3], (N_REP, N_DOM), 0, 2)
    count_zero = jnp.where(swapped == 1, loads - first_count, first_count)
    count_one = loads - count_zero
    counts = jnp.stack([count_zero.T, count_one.T], axis=0).astype(jnp.int32)
    column_keys = jax.random.split(keys[4], 2 * N_DOM * N_REP)
    columns = jax.vmap(lambda sub: jax.random.permutation(sub, LMAX))(column_keys).reshape(2, N_DOM, N_REP, LMAX).astype(jnp.int32)
    return (columns, counts)


def draw_columns(key, part):
    return plan_lists(key)[0]


def draw_counts(key, part):
    return plan_lists(key)[1]


def level_of(stream_key, extent, cuts, least, top_value):
    level = 1.0
    for axis_at, blocks in cuts:
        steps = jax.random.uniform(jax.random.fold_in(jax.random.fold_in(stream_key, 6), axis_at), (blocks,), jnp.float32, least / len(cuts), top_value / len(cuts))
        level = level * jnp.repeat(jnp.exp(steps), extent[axis_at] // blocks).reshape((-1,) + (1,) * (len(extent) - 1 - axis_at))
    return level


def centred(key, extent, deviation, reach, pieces=(), held_as=jnp.bfloat16):
    entries = deviation * jax.random.normal(key, extent, jnp.float32)
    if pieces:
        entries = entries * level_of(key, extent, pieces, -0.22, 0.18)
    return jnp.clip(entries, -reach, reach).astype(held_as)


def setup_inputs(seed: int = 0) -> dict:
    key_of = jax.random.split(jax.random.key(seed), 6)
    features = centred(key_of[0], (SRC, FEAT), 1.0, 6.0, ((0, 32),))
    tiles = jnp.clip(0.039794922 * jax.random.uniform(key_of[1], (N_DOM, N_REP, WORK, TILE, TILE), jnp.float32) ** level_of(key_of[1], (N_DOM, N_REP, WORK, TILE, TILE), ((0, 32), (1, 4), (3, 8)), -0.2, 0.2), 0.0, 0.039794922).astype(jnp.bfloat16)
    columns = draw_columns(jax.random.fold_in(key_of[5], 71), 0)
    counts = draw_counts(jax.random.fold_in(key_of[5], 71), 0)
    weights = centred(key_of[4], (2, FEAT, FEAT), FEAT ** -0.5, 0.21875)
    return dict(features=features, tiles=tiles, columns=columns, counts=counts, weights=weights)


def combine_rows(strips, panel_ids, labels, relation, present, panels, weights):
    chosen = jnp.take(panels, panel_ids, axis=0).astype(jnp.float32)
    products = jnp.einsum("kst,ktf->ksf", strips.astype(jnp.float32), chosen, precision=lax.Precision.HIGHEST)
    relation_kinds = jnp.arange(2, dtype=jnp.int32)
    member = present[None, None, :] & (labels[:, None, None] == labels[None, None, :]) & (relation[None, None, :] == relation_kinds[None, :, None])
    group_sums = jnp.einsum("krj,jsf->krsf", member.astype(jnp.float32), products, precision=lax.Precision.HIGHEST).astype(jnp.bfloat16)
    mixed_rows = jnp.einsum("krsf,rfg->ksg", group_sums.astype(jnp.float32), weights.astype(jnp.float32), precision=lax.Precision.HIGHEST).astype(jnp.bfloat16)
    entry_index = jnp.arange(labels.shape[0], dtype=jnp.int32)
    earlier = present[None, :] & (labels[:, None] == labels[None, :]) & (entry_index[None, :] < entry_index[:, None])
    leading = present & jnp.logical_not(jnp.any(earlier, axis=1))
    return mixed_rows, leading


def reference(features, tiles, columns, counts, weights):
    panels_all = features.reshape(N_REP, N_GRP, TILE, FEAT)
    relation = jnp.repeat(jnp.arange(2, dtype=jnp.int32), LMAX)
    position = jnp.tile(jnp.arange(LMAX, dtype=jnp.int32), 2)
    loads = (counts[0] + counts[1]).astype(jnp.int32)
    starts = (jnp.cumsum(loads, axis=0) - loads).astype(jnp.int32)

    def one_block(block_index):
        owner_index = block_index // N_REP
        column_group = block_index % N_REP
        limits = counts[:, owner_index, column_group].astype(jnp.int32)
        places = (starts[owner_index, column_group] + relation * limits[0] + position).astype(jnp.int32)
        labels = (places % N_DOM).astype(jnp.int32)
        slot_ids = jnp.minimum(places // N_DOM, WORK - 1).astype(jnp.int32)
        strips = tiles[labels, column_group, slot_ids]
        panel_ids = columns[:, owner_index, column_group].reshape(2 * LMAX).astype(jnp.int32)
        present = position < jnp.where(relation == 0, limits[0], limits[1])
        mixed_rows, leading = combine_rows(strips, panel_ids, labels, relation, present, panels_all[column_group], weights)
        return jnp.sum(jnp.where(leading[:, None, None], mixed_rows.astype(jnp.float32), jnp.zeros((), jnp.float32)), axis=0)

    blocks = lax.map(one_block, jnp.arange(N_DOM * N_REP, dtype=jnp.int32))
    total = jnp.sum(blocks.reshape(N_DOM, N_REP, TILE, FEAT), axis=1)
    return total.reshape(N_DOM * TILE, FEAT).astype(jnp.bfloat16)
```

```python
import jax
import jax.numpy as jnp
from jax import lax
from jax.sharding import PartitionSpec as P


def on_device(features, tiles, columns, counts, weights):
    slot_count = tiles.shape[2]
    strip_rows = tiles.shape[3]
    tile_cols = tiles.shape[4]
    list_len = columns.shape[3]
    feat_dim = features.shape[1]
    owners_count = lax.axis_size("dom")
    me = lax.axis_index("dom")
    column_group = lax.axis_index("rep")
    max_load = 2 * list_len

    gathered = lax.all_gather(features, "grp", axis=0, tiled=True)
    panels = gathered.reshape(list_len * tile_cols, feat_dim)

    first_counts = counts[0][:, column_group]
    group_loads = first_counts + counts[1][:, column_group]
    owner_starts = jnp.cumsum(group_loads) - group_loads

    strips = tiles.reshape(slot_count, strip_rows, tile_cols)
    owner_slot = (owner_starts - me + owners_count - 1) // owners_count
    owner_slot = jnp.clip(owner_slot, 0, slot_count - 1)
    owner_place = me + owner_slot * owners_count
    owner_has = (owner_place >= owner_starts) & (owner_place < owner_starts + group_loads)
    outgoing = jnp.where(owner_has[:, None, None], jnp.take(strips, owner_slot, axis=0), jnp.zeros((), strips.dtype))
    incoming = lax.all_to_all(outgoing, "dom", split_axis=0, concat_axis=0, tiled=True)

    my_start = owner_starts[me]
    my_load = group_loads[me]
    my_first = first_counts[me]
    entry = jnp.arange(max_load, dtype=jnp.int32)
    entry_valid = entry < my_load
    entry_worker = (my_start + entry) % owners_count
    entry_rel = (entry >= my_first).astype(jnp.int32)
    entry_k = jnp.clip(entry - entry_rel * my_first, 0, list_len - 1)
    my_columns = columns[:, me, column_group, :]
    entry_col = my_columns[entry_rel, entry_k]
    blocks = jnp.take(incoming, entry_worker, axis=0)
    blocks = jnp.where(entry_valid[:, None, None], blocks, jnp.zeros((), blocks.dtype))
    col_hot = entry_col[:, None] == jnp.arange(list_len, dtype=jnp.int32)[None, :]
    placed = jnp.where(col_hot[:, None, :, None], blocks[:, :, None, :], jnp.zeros((), blocks.dtype))
    placed = placed.reshape(max_load * strip_rows, list_len * tile_cols)
    products = jnp.dot(placed, panels, preferred_element_type=jnp.float32).astype(jnp.bfloat16)
    products = products.reshape(max_load, strip_rows, feat_dim)
    rel_hot = entry_rel[:, None] == jnp.arange(2, dtype=jnp.int32)[None, :]
    split = jnp.where(rel_hot[:, None, :, None], products[:, :, None, :], jnp.zeros((), products.dtype))
    split = split.reshape(max_load * strip_rows, 2 * feat_dim)
    terms = jnp.dot(split, weights.reshape(2 * feat_dim, feat_dim), preferred_element_type=jnp.float32)
    terms = terms.astype(jnp.bfloat16).reshape(max_load, strip_rows, feat_dim)
    partial_value = jnp.sum(terms.astype(jnp.float32), axis=0)
    result = lax.psum_scatter(partial_value, "rep", scatter_dimension=0, tiled=True)
    return result.astype(jnp.bfloat16)


def solution(mesh):
    return jax.shard_map(
        on_device,
        mesh=mesh,
        in_specs=(P(("rep", "grp"), None), P("dom", "rep", None, "grp", None), P(), P(), P()),
        out_specs=P(("dom", "grp", "rep"), None),
        check_vma=False,
    )
```

```python
import jax
import jax.numpy as jnp
from jax import lax
from jax.sharding import PartitionSpec as P


def on_device(features, tiles, columns, counts, weights):
    slot_count = tiles.shape[2]
    strip_rows = tiles.shape[3]
    tile_cols = tiles.shape[4]
    list_len = columns.shape[3]
    feat_dim = features.shape[1]
    owners_count = lax.axis_size("dom")
    me = lax.axis_index("dom")
    column_group = lax.axis_index("rep")
    max_load = 2 * list_len

    gathered = lax.all_gather(features, "grp", axis=0, tiled=True)
    panels = gathered.reshape(list_len * tile_cols, feat_dim)

    first_counts = counts[0][:, column_group]
    group_loads = first_counts + counts[1][:, column_group]
    owner_starts = jnp.cumsum(group_loads) - group_loads

    strips = tiles.reshape(slot_count, strip_rows, tile_cols)
    owner_slot = (owner_starts - me + owners_count - 1) // owners_count
    owner_slot = jnp.clip(owner_slot, 0, slot_count - 1)
    owner_place = me + owner_slot * owners_count
    owner_has = (owner_place >= owner_starts) & (owner_place < owner_starts + group_loads)
    outgoing = jnp.where(owner_has[:, None, None], jnp.take(strips, owner_slot, axis=0), jnp.zeros((), strips.dtype))
    incoming = lax.all_to_all(outgoing, "dom", split_axis=0, concat_axis=0, tiled=True)

    my_start = owner_starts[me]
    my_load = group_loads[me]
    my_first = first_counts[me]
    entry = jnp.arange(max_load, dtype=jnp.int32)
    entry_valid = entry < my_load
    entry_worker = (my_start + entry) % owners_count
    entry_rel = (entry >= my_first).astype(jnp.int32)
    entry_k = jnp.clip(entry - entry_rel * my_first, 0, list_len - 1)
    my_columns = columns[:, me, column_group, :]
    entry_col = my_columns[entry_rel, entry_k]
    blocks = jnp.take(incoming, entry_worker, axis=0)
    blocks = jnp.where(entry_valid[:, None, None], blocks, jnp.zeros((), blocks.dtype))
    col_hot = entry_col[:, None] == jnp.arange(list_len, dtype=jnp.int32)[None, :]
    placed = jnp.where(col_hot[:, None, :, None], blocks[:, :, None, :], jnp.zeros((), blocks.dtype))
    placed = placed.reshape(max_load * strip_rows, list_len * tile_cols)
    products = jnp.dot(placed, panels, preferred_element_type=jnp.float32).astype(jnp.bfloat16)
    products = products.reshape(max_load, strip_rows, feat_dim)
    rel_hot = entry_rel[:, None] == jnp.arange(2, dtype=jnp.int32)[None, :]
    split = jnp.where(rel_hot[:, None, :, None], products[:, :, None, :], jnp.zeros((), products.dtype))
    split = split.reshape(max_load * strip_rows, 2 * feat_dim)
    terms = jnp.dot(split, weights.reshape(2 * feat_dim, feat_dim), preferred_element_type=jnp.float32)
    terms = terms.astype(jnp.bfloat16).reshape(max_load, strip_rows, feat_dim)
    partial_value = jnp.sum(terms.astype(jnp.float32), axis=0)
    rep_count = lax.axis_size("rep")
    pieces = partial_value.reshape(rep_count, strip_rows // rep_count, feat_dim)
    pieces = lax.all_to_all(pieces, "rep", split_axis=0, concat_axis=0, tiled=True)
    return jnp.sum(pieces, axis=0).astype(jnp.bfloat16)


def solution(mesh):
    return jax.shard_map(
        on_device,
        mesh=mesh,
        in_specs=(P(("rep", "grp"), None), P("dom", "rep", None, "grp", None), P(), P(), P()),
        out_specs=P(("dom", "grp", "rep"), None),
        check_vma=False,
    )
```

```python
import jax
import jax.numpy as jnp
from jax import lax
from jax.sharding import PartitionSpec as P


def on_device(features, tiles, columns, counts, weights):
    slot_count = tiles.shape[2]
    strip_rows = tiles.shape[3]
    tile_cols = tiles.shape[4]
    list_len = columns.shape[3]
    feat_dim = features.shape[1]
    owners_count = lax.axis_size("dom")
    me = lax.axis_index("dom")
    column_group = lax.axis_index("rep")
    max_load = 2 * list_len

    grp_count = lax.axis_size("grp")
    my_grp = lax.axis_index("grp")
    parity = me % 2
    half = feat_dim // 2
    mine = lax.dynamic_slice_in_dim(features, parity * half, half, axis=1)
    up = [(i, (i + 1) % grp_count) for i in range(grp_count)]
    down = [(i, (i - 1) % grp_count) for i in range(grp_count)]
    pieces = [None] * grp_count
    pieces[0] = mine
    fwd = mine
    bwd = mine
    reach = grp_count // 2
    for t in range(1, reach):
        fwd = lax.ppermute(fwd, "grp", up)
        bwd = lax.ppermute(bwd, "grp", down)
        pieces[grp_count - t] = fwd
        pieces[t] = bwd
    rows_half = tile_cols // 2
    far_a = lax.ppermute(fwd[:rows_half], "grp", up)
    far_b = lax.ppermute(bwd[rows_half:], "grp", down)
    pieces[reach] = jnp.concatenate([far_a, far_b], axis=0)
    my_panels = jnp.stack(pieces, axis=0)
    pairs = [(i, i ^ 1) for i in range(owners_count)]
    other_panels = lax.ppermute(my_panels, "dom", pairs)
    low = jnp.where(parity == 0, my_panels, other_panels)
    high = jnp.where(parity == 0, other_panels, my_panels)
    panels = jnp.concatenate([low, high], axis=2).reshape(list_len * tile_cols, feat_dim)

    first_counts = counts[0][:, column_group]
    group_loads = first_counts + counts[1][:, column_group]
    owner_starts = jnp.cumsum(group_loads) - group_loads

    strips = tiles.reshape(slot_count, strip_rows, tile_cols)
    owner_slot = (owner_starts - me + owners_count - 1) // owners_count
    owner_slot = jnp.clip(owner_slot, 0, slot_count - 1)
    owner_place = me + owner_slot * owners_count
    owner_has = (owner_place >= owner_starts) & (owner_place < owner_starts + group_loads)
    outgoing = jnp.where(owner_has[:, None, None], jnp.take(strips, owner_slot, axis=0), jnp.zeros((), strips.dtype))
    incoming = lax.all_to_all(outgoing, "dom", split_axis=0, concat_axis=0, tiled=True)

    my_start = owner_starts[me]
    my_load = group_loads[me]
    my_first = first_counts[me]
    entry = jnp.arange(max_load, dtype=jnp.int32)
    entry_valid = entry < my_load
    entry_worker = (my_start + entry) % owners_count
    entry_rel = (entry >= my_first).astype(jnp.int32)
    entry_k = jnp.clip(entry - entry_rel * my_first, 0, list_len - 1)
    my_columns = columns[:, me, column_group, :]
    entry_col = (my_columns[entry_rel, entry_k] - my_grp) % grp_count
    blocks = jnp.take(incoming, entry_worker, axis=0)
    blocks = jnp.where(entry_valid[:, None, None], blocks, jnp.zeros((), blocks.dtype))
    col_hot = entry_col[:, None] == jnp.arange(list_len, dtype=jnp.int32)[None, :]
    placed = jnp.where(col_hot[:, None, :, None], blocks[:, :, None, :], jnp.zeros((), blocks.dtype))
    placed = placed.reshape(max_load * strip_rows, list_len * tile_cols)
    products = jnp.dot(placed, panels, preferred_element_type=jnp.float32).astype(jnp.bfloat16)
    products = products.reshape(max_load, strip_rows, feat_dim)
    rel_hot = entry_rel[:, None] == jnp.arange(2, dtype=jnp.int32)[None, :]
    split = jnp.where(rel_hot[:, None, :, None], products[:, :, None, :], jnp.zeros((), products.dtype))
    split = split.reshape(max_load * strip_rows, 2 * feat_dim)
    terms = jnp.dot(split, weights.reshape(2 * feat_dim, feat_dim), preferred_element_type=jnp.float32)
    terms = terms.astype(jnp.bfloat16).reshape(max_load, strip_rows, feat_dim)
    partial_value = jnp.sum(terms.astype(jnp.float32), axis=0)
    rep_count = lax.axis_size("rep")
    pieces = partial_value.reshape(rep_count, strip_rows // rep_count, feat_dim)
    pieces = lax.all_to_all(pieces, "rep", split_axis=0, concat_axis=0, tiled=True)
    return jnp.sum(pieces, axis=0).astype(jnp.bfloat16)


def solution(mesh):
    return jax.shard_map(
        on_device,
        mesh=mesh,
        in_specs=(P(("rep", "grp"), None), P("dom", "rep", None, "grp", None), P(), P(), P()),
        out_specs=P(("dom", "grp", "rep"), None),
        check_vma=False,
    )
```

```python
import jax
import jax.numpy as jnp
from jax import lax
from jax.sharding import PartitionSpec as P


def on_device(features, tiles, columns, counts, weights):
    slot_count = tiles.shape[2]
    strip_rows = tiles.shape[3]
    tile_cols = tiles.shape[4]
    list_len = columns.shape[3]
    feat_dim = features.shape[1]
    chip_count = lax.axis_size("z")
    core_count = lax.axis_size("core")
    owners_count = chip_count * core_count
    my_core = lax.axis_index("core")
    me = lax.axis_index("z") * core_count + my_core
    column_group = lax.axis_index("rep")
    max_load = 2 * list_len

    swap = [(0, 1), (1, 0)]
    half = feat_dim // core_count
    mine = lax.dynamic_slice_in_dim(features, my_core * half, half, axis=1)
    mine = lax.all_gather(mine, "grp", axis=0, tiled=True)
    other = lax.ppermute(mine, "core", swap)
    low = jnp.where(my_core == 0, mine, other)
    high = jnp.where(my_core == 0, other, mine)
    panels = jnp.concatenate([low, high], axis=1)

    first_counts = counts[0][:, column_group]
    group_loads = first_counts + counts[1][:, column_group]
    owner_starts = jnp.cumsum(group_loads) - group_loads

    strips = tiles.reshape(slot_count, strip_rows, tile_cols)
    chip_loads = group_loads.reshape(chip_count, core_count).sum(axis=1)
    chip_starts = owner_starts.reshape(chip_count, core_count)[:, 0]
    chip_slot = (chip_starts - me + owners_count - 1) // owners_count
    chip_slot = jnp.clip(chip_slot, 0, slot_count - 1)
    chip_place = me + chip_slot * owners_count
    chip_has = (chip_place >= chip_starts) & (chip_place < chip_starts + chip_loads)
    outgoing = jnp.where(chip_has[:, None, None], jnp.take(strips, chip_slot, axis=0), jnp.zeros((), strips.dtype))
    from_chips = lax.all_to_all(outgoing, "z", split_axis=0, concat_axis=0, tiled=True)
    from_sibling = lax.ppermute(from_chips, "core", swap)
    from_core0 = jnp.where(my_core == 0, from_chips, from_sibling)
    from_core1 = jnp.where(my_core == 0, from_sibling, from_chips)
    incoming = jnp.stack([from_core0, from_core1], axis=1).reshape(owners_count, strip_rows, tile_cols)

    my_start = owner_starts[me]
    my_load = group_loads[me]
    my_first = first_counts[me]
    entry = jnp.arange(max_load, dtype=jnp.int32)
    entry_valid = entry < my_load
    entry_worker = (my_start + entry) % owners_count
    entry_rel = (entry >= my_first).astype(jnp.int32)
    entry_k = jnp.clip(entry - entry_rel * my_first, 0, list_len - 1)
    my_columns = columns[:, me, column_group, :]
    entry_col = my_columns[entry_rel, entry_k]
    blocks = jnp.take(incoming, entry_worker, axis=0)
    blocks = jnp.where(entry_valid[:, None, None], blocks, jnp.zeros((), blocks.dtype))
    col_hot = entry_col[:, None] == jnp.arange(list_len, dtype=jnp.int32)[None, :]
    placed = jnp.where(col_hot[:, None, :, None], blocks[:, :, None, :], jnp.zeros((), blocks.dtype))
    placed = placed.reshape(max_load * strip_rows, list_len * tile_cols)
    products = jnp.dot(placed, panels, preferred_element_type=jnp.float32).astype(jnp.bfloat16)
    products = products.reshape(max_load, strip_rows, feat_dim)
    rel_hot = entry_rel[:, None] == jnp.arange(2, dtype=jnp.int32)[None, :]
    split = jnp.where(rel_hot[:, None, :, None], products[:, :, None, :], jnp.zeros((), products.dtype))
    split = split.reshape(max_load * strip_rows, 2 * feat_dim)
    terms = jnp.dot(split, weights.reshape(2 * feat_dim, feat_dim), preferred_element_type=jnp.float32)
    terms = terms.astype(jnp.bfloat16).reshape(max_load, strip_rows, feat_dim)
    partial_value = jnp.sum(terms.astype(jnp.float32), axis=0)
    rep_count = lax.axis_size("rep")
    pieces = partial_value.reshape(rep_count, strip_rows // rep_count, feat_dim)
    pieces = lax.all_to_all(pieces, "rep", split_axis=0, concat_axis=0, tiled=True)
    return jnp.sum(pieces, axis=0).astype(jnp.bfloat16)


def solution(mesh):
    dom_size, grp_size, rep_size = mesh.devices.shape
    split = jax.sharding.Mesh(
        mesh.devices.reshape(dom_size // 2, 2, grp_size, rep_size), ("z", "core", "grp", "rep")
    )
    return jax.shard_map(
        on_device,
        mesh=split,
        in_specs=(P(("rep", "grp"), None), P(("z", "core"), "rep", None, "grp", None), P(), P(), P()),
        out_specs=P(("z", "core", "grp", "rep"), None),
        check_vma=False,
    )
```

```python
import jax
import jax.numpy as jnp
from jax import lax
from jax.sharding import PartitionSpec as P


def on_device(features, tiles, columns, counts, weights):
    slot_count = tiles.shape[2]
    strip_rows = tiles.shape[3]
    tile_cols = tiles.shape[4]
    list_len = columns.shape[3]
    feat_dim = features.shape[1]
    chip_count = lax.axis_size("z")
    core_count = lax.axis_size("core")
    owners_count = chip_count * core_count
    my_core = lax.axis_index("core")
    me = lax.axis_index("z") * core_count + my_core
    column_group = lax.axis_index("rep")
    max_load = 2 * list_len

    swap = [(0, 1), (1, 0)]
    half = feat_dim // core_count
    grp_count = lax.axis_size("grp")
    mine = lax.dynamic_slice_in_dim(features, my_core * half, half, axis=1)
    my_grp = lax.axis_index("grp")
    pieces = [mine] + [
        lax.ppermute(mine, "grp", [(i, (i + grp_count - r) % grp_count) for i in range(grp_count)])
        for r in range(1, grp_count)
    ]
    panels = jnp.concatenate(pieces, axis=0)

    first_counts = counts[0][:, column_group]
    group_loads = first_counts + counts[1][:, column_group]
    owner_starts = jnp.cumsum(group_loads) - group_loads

    strips = tiles.reshape(slot_count, strip_rows, tile_cols)
    chip_loads = group_loads.reshape(chip_count, core_count).sum(axis=1)
    chip_starts = owner_starts.reshape(chip_count, core_count)[:, 0]
    chip_slot = (chip_starts - me + owners_count - 1) // owners_count
    chip_slot = jnp.clip(chip_slot, 0, slot_count - 1)
    chip_place = me + chip_slot * owners_count
    chip_has = (chip_place >= chip_starts) & (chip_place < chip_starts + chip_loads)
    outgoing = jnp.where(chip_has[:, None, None], jnp.take(strips, chip_slot, axis=0), jnp.zeros((), strips.dtype))
    from_chips = lax.all_to_all(outgoing, "z", split_axis=0, concat_axis=0, tiled=True)
    from_sibling = lax.ppermute(from_chips, "core", swap)
    from_core0 = jnp.where(my_core == 0, from_chips, from_sibling)
    from_core1 = jnp.where(my_core == 0, from_sibling, from_chips)
    incoming = jnp.stack([from_core0, from_core1], axis=1).reshape(owners_count, strip_rows, tile_cols)

    chip_first = me - my_core
    owner_ids = chip_first + jnp.arange(core_count, dtype=jnp.int32)
    entry = jnp.arange(max_load, dtype=jnp.int32)[None, :]
    starts = owner_starts[owner_ids][:, None]
    loads = group_loads[owner_ids][:, None]
    firsts = first_counts[owner_ids][:, None]
    entry_valid = entry < loads
    entry_worker = (starts + entry) % owners_count
    entry_rel = (entry >= firsts).astype(jnp.int32)
    entry_k = jnp.clip(entry - entry_rel * firsts, 0, list_len - 1)
    pair_columns = columns[:, owner_ids, column_group, :]
    entry_col = (pair_columns[entry_rel, jnp.arange(core_count)[:, None], entry_k] - my_grp) % grp_count
    entry_valid = entry_valid.reshape(-1)
    entry_rel = entry_rel.reshape(-1)
    entry_col = entry_col.reshape(-1)
    blocks = jnp.take(incoming, entry_worker.reshape(-1), axis=0)
    blocks = jnp.where(entry_valid[:, None, None], blocks, jnp.zeros((), blocks.dtype))
    n_entries = core_count * max_load
    col_hot = entry_col[:, None] == jnp.arange(list_len, dtype=jnp.int32)[None, :]
    placed = jnp.where(col_hot[:, None, :, None], blocks[:, :, None, :], jnp.zeros((), blocks.dtype))
    placed = placed.reshape(n_entries * strip_rows, list_len * tile_cols)
    products = jnp.dot(placed, panels, preferred_element_type=jnp.float32).astype(jnp.bfloat16)
    products = products.reshape(n_entries, strip_rows, half)
    rel_hot = entry_rel[:, None] == jnp.arange(2, dtype=jnp.int32)[None, :]
    split = jnp.where(rel_hot[:, None, :, None], products[:, :, None, :], jnp.zeros((), products.dtype))
    split = split.reshape(n_entries * strip_rows, 2 * half)
    my_weights = lax.dynamic_slice_in_dim(weights, my_core * half, half, axis=1)
    terms = jnp.dot(split, my_weights.reshape(2 * half, feat_dim), preferred_element_type=jnp.float32)
    partial_value = jnp.sum(terms.reshape(core_count, max_load, strip_rows, feat_dim), axis=1)
    rep_count = lax.axis_size("rep")
    pieces = partial_value.reshape(core_count * rep_count, strip_rows // rep_count, feat_dim)
    pieces = lax.all_to_all(pieces, ("core", "rep"), split_axis=0, concat_axis=0, tiled=True)
    return jnp.sum(pieces, axis=0).astype(jnp.bfloat16)


def solution(mesh):
    dom_size, grp_size, rep_size = mesh.devices.shape
    split = jax.sharding.Mesh(
        mesh.devices.reshape(dom_size // 2, 2, grp_size, rep_size), ("z", "core", "grp", "rep")
    )
    return jax.shard_map(
        on_device,
        mesh=split,
        in_specs=(P(("rep", "grp"), None), P(("z", "core"), "rep", None, "grp", None), P(), P(), P()),
        out_specs=P(("z", "core", "grp", "rep"), None),
        check_vma=False,
    )
```

```python
import jax
import jax.numpy as jnp
from jax import lax
from jax.sharding import PartitionSpec as P


def on_device(features, tiles, columns, counts, weights):
    slot_count = tiles.shape[2]
    strip_rows = tiles.shape[3]
    tile_cols = tiles.shape[4]
    list_len = columns.shape[3]
    feat_dim = features.shape[1]
    owners_count = lax.axis_size("dom")
    me = lax.axis_index("dom")
    column_group = lax.axis_index("rep")
    max_load = 2 * list_len

    gathered = lax.all_gather(features, "grp", axis=0, tiled=True)
    panels = gathered.reshape(list_len * tile_cols, feat_dim)

    first_counts = counts[0][:, column_group]
    group_loads = first_counts + counts[1][:, column_group]
    owner_starts = jnp.cumsum(group_loads) - group_loads

    strips = tiles.reshape(slot_count, strip_rows, tile_cols)
    owner_slot = (owner_starts - me + owners_count - 1) // owners_count
    owner_slot = jnp.clip(owner_slot, 0, slot_count - 1)
    owner_place = me + owner_slot * owners_count
    owner_has = (owner_place >= owner_starts) & (owner_place < owner_starts + group_loads)
    outgoing = jnp.where(owner_has[:, None, None], jnp.take(strips, owner_slot, axis=0), jnp.zeros((), strips.dtype))
    incoming = lax.all_to_all(outgoing, "dom", split_axis=0, concat_axis=0, tiled=True)

    my_start = owner_starts[me]
    my_load = group_loads[me]
    my_first = first_counts[me]
    entry = jnp.arange(max_load, dtype=jnp.int32)
    entry_valid = entry < my_load
    entry_worker = (my_start + entry) % owners_count
    entry_rel = (entry >= my_first).astype(jnp.int32)
    entry_k = jnp.clip(entry - entry_rel * my_first, 0, list_len - 1)
    my_columns = columns[:, me, column_group, :]
    entry_col = my_columns[entry_rel, entry_k]
    blocks = jnp.take(incoming, entry_worker, axis=0)
    blocks = jnp.where(entry_valid[:, None, None], blocks, jnp.zeros((), blocks.dtype))
    rows = max_load * strip_rows
    row_col = jnp.repeat(entry_col, strip_rows)
    lane_panel = jnp.arange(list_len * tile_cols, dtype=jnp.int32) // tile_cols
    placed = jnp.tile(blocks.reshape(rows, tile_cols), (1, list_len))
    placed = jnp.where(row_col[:, None] == lane_panel[None, :], placed, jnp.zeros((), placed.dtype))
    products = jnp.dot(placed, panels, preferred_element_type=jnp.float32).astype(jnp.bfloat16)
    row_rel = jnp.repeat(entry_rel, strip_rows)[:, None]
    zero = jnp.zeros((), products.dtype)
    terms = jnp.dot(jnp.where(row_rel == 0, products, zero), weights[0], preferred_element_type=jnp.float32)
    terms = terms + jnp.dot(jnp.where(row_rel == 1, products, zero), weights[1], preferred_element_type=jnp.float32)
    terms = terms.astype(jnp.bfloat16).reshape(max_load, strip_rows, feat_dim)
    partial_value = jnp.sum(terms.astype(jnp.float32), axis=0)
    rep_count = lax.axis_size("rep")
    pieces = partial_value.reshape(rep_count, strip_rows // rep_count, feat_dim)
    pieces = lax.all_to_all(pieces, "rep", split_axis=0, concat_axis=0, tiled=True)
    return jnp.sum(pieces, axis=0).astype(jnp.bfloat16)


def solution(mesh):
    return jax.shard_map(
        on_device,
        mesh=mesh,
        in_specs=(P(("rep", "grp"), None), P("dom", "rep", None, "grp", None), P(), P(), P()),
        out_specs=P(("dom", "grp", "rep"), None),
        check_vma=False,
    )
```

```python
import jax
import jax.numpy as jnp
from jax import lax
from jax.sharding import PartitionSpec as P


def on_device(features, tiles, columns, counts, weights):
    slot_count = tiles.shape[2]
    strip_rows = tiles.shape[3]
    tile_cols = tiles.shape[4]
    list_len = columns.shape[3]
    feat_dim = features.shape[1]
    chip_count = lax.axis_size("z")
    core_count = lax.axis_size("core")
    owners_count = chip_count * core_count
    my_core = lax.axis_index("core")
    me = lax.axis_index("z") * core_count + my_core
    column_group = lax.axis_index("rep")
    max_load = 2 * list_len

    swap = [(0, 1), (1, 0)]
    half = feat_dim // core_count
    mine = lax.dynamic_slice_in_dim(features, my_core * half, half, axis=1)
    panels = lax.all_gather(mine, "grp", axis=0, tiled=True)

    first_counts = counts[0][:, column_group]
    group_loads = first_counts + counts[1][:, column_group]
    owner_starts = jnp.cumsum(group_loads) - group_loads

    strips = tiles.reshape(slot_count, strip_rows, tile_cols)
    chip_loads = group_loads.reshape(chip_count, core_count).sum(axis=1)
    chip_starts = owner_starts.reshape(chip_count, core_count)[:, 0]
    chip_slot = (chip_starts - me + owners_count - 1) // owners_count
    chip_slot = jnp.clip(chip_slot, 0, slot_count - 1)
    chip_place = me + chip_slot * owners_count
    chip_has = (chip_place >= chip_starts) & (chip_place < chip_starts + chip_loads)
    outgoing = jnp.where(chip_has[:, None, None], jnp.take(strips, chip_slot, axis=0), jnp.zeros((), strips.dtype))
    from_chips = lax.all_to_all(outgoing, "z", split_axis=0, concat_axis=0, tiled=True)
    from_sibling = lax.ppermute(from_chips, "core", swap)
    from_core0 = jnp.where(my_core == 0, from_chips, from_sibling)
    from_core1 = jnp.where(my_core == 0, from_sibling, from_chips)
    incoming = jnp.stack([from_core0, from_core1], axis=1).reshape(owners_count, strip_rows, tile_cols)

    chip_first = me - my_core
    owner_ids = chip_first + jnp.arange(core_count, dtype=jnp.int32)
    entry = jnp.arange(max_load, dtype=jnp.int32)[None, :]
    starts = owner_starts[owner_ids][:, None]
    loads = group_loads[owner_ids][:, None]
    firsts = first_counts[owner_ids][:, None]
    entry_valid = entry < loads
    entry_worker = (starts + entry) % owners_count
    entry_rel = (entry >= firsts).astype(jnp.int32)
    entry_k = jnp.clip(entry - entry_rel * firsts, 0, list_len - 1)
    pair_columns = columns[:, owner_ids, column_group, :]
    entry_col = pair_columns[entry_rel, jnp.arange(core_count)[:, None], entry_k]
    entry_valid = entry_valid.reshape(-1)
    entry_rel = entry_rel.reshape(-1)
    entry_col = entry_col.reshape(-1)
    blocks = jnp.take(incoming, entry_worker.reshape(-1), axis=0)
    blocks = jnp.where(entry_valid[:, None, None], blocks, jnp.zeros((), blocks.dtype))
    n_entries = core_count * max_load
    rows = n_entries * strip_rows
    row_col = jnp.repeat(entry_col, strip_rows)
    lane_panel = jnp.arange(list_len * tile_cols, dtype=jnp.int32) // tile_cols
    placed = jnp.tile(blocks.reshape(rows, tile_cols), (1, list_len))
    placed = jnp.where(row_col[:, None] == lane_panel[None, :], placed, jnp.zeros((), placed.dtype))
    products = jnp.dot(placed, panels, preferred_element_type=jnp.float32).astype(jnp.bfloat16)
    row_rel = jnp.repeat(entry_rel, strip_rows)[:, None]
    zero = jnp.zeros((), products.dtype)
    my_weights = lax.dynamic_slice_in_dim(weights, my_core * half, half, axis=1)
    terms = jnp.dot(jnp.where(row_rel == 0, products, zero), my_weights[0], preferred_element_type=jnp.float32)
    terms = terms + jnp.dot(jnp.where(row_rel == 1, products, zero), my_weights[1], preferred_element_type=jnp.float32)
    partial_value = jnp.sum(terms.reshape(core_count, max_load, strip_rows, feat_dim), axis=1)
    rep_count = lax.axis_size("rep")
    pieces = partial_value.reshape(core_count * rep_count, strip_rows // rep_count, feat_dim)
    pieces = lax.all_to_all(pieces, ("core", "rep"), split_axis=0, concat_axis=0, tiled=True)
    return jnp.sum(pieces, axis=0).astype(jnp.bfloat16)


def solution(mesh):
    dom_size, grp_size, rep_size = mesh.devices.shape
    split = jax.sharding.Mesh(
        mesh.devices.reshape(dom_size // 2, 2, grp_size, rep_size), ("z", "core", "grp", "rep")
    )
    return jax.shard_map(
        on_device,
        mesh=split,
        in_specs=(P(("rep", "grp"), None), P(("z", "core"), "rep", None, "grp", None), P(), P(), P()),
        out_specs=P(("z", "core", "grp", "rep"), None),
        check_vma=False,
    )
```

```python
import jax
import jax.numpy as jnp
from jax import lax
from jax.sharding import PartitionSpec as P


def on_device(features, tiles, columns, counts, weights):
    slot_count = tiles.shape[2]
    strip_rows = tiles.shape[3]
    tile_cols = tiles.shape[4]
    list_len = columns.shape[3]
    feat_dim = features.shape[1]
    chip_count = lax.axis_size("z")
    core_count = lax.axis_size("core")
    owners_count = chip_count * core_count
    my_core = lax.axis_index("core")
    me = lax.axis_index("z") * core_count + my_core
    column_group = lax.axis_index("rep")
    max_load = 2 * list_len

    swap = [(0, 1), (1, 0)]
    half = feat_dim // core_count
    mine = lax.dynamic_slice_in_dim(features, my_core * half, half, axis=1)
    panels = lax.all_gather(mine, "grp", axis=0, tiled=True)

    first_counts = counts[0][:, column_group]
    group_loads = first_counts + counts[1][:, column_group]
    owner_starts = jnp.cumsum(group_loads) - group_loads

    strips = tiles.reshape(slot_count, strip_rows, tile_cols)
    chip_loads = group_loads.reshape(chip_count, core_count).sum(axis=1)
    chip_starts = owner_starts.reshape(chip_count, core_count)[:, 0]
    chip_slot = (chip_starts - me + owners_count - 1) // owners_count
    chip_slot = jnp.clip(chip_slot, 0, slot_count - 1)
    chip_place = me + chip_slot * owners_count
    chip_has = (chip_place >= chip_starts) & (chip_place < chip_starts + chip_loads)
    outgoing = jnp.where(chip_has[:, None, None], jnp.take(strips, chip_slot, axis=0), jnp.zeros((), strips.dtype))
    from_chips = lax.all_to_all(outgoing, "z", split_axis=0, concat_axis=0, tiled=True)
    from_sibling = lax.ppermute(from_chips, "core", swap)
    from_core0 = jnp.where(my_core == 0, from_chips, from_sibling)
    from_core1 = jnp.where(my_core == 0, from_sibling, from_chips)
    incoming = jnp.stack([from_core0, from_core1], axis=1).reshape(owners_count, strip_rows, tile_cols)

    chip_first = me - my_core
    owner_ids = chip_first + jnp.arange(core_count, dtype=jnp.int32)
    starts = owner_starts[owner_ids]
    firsts = first_counts[owner_ids]
    pair_columns = columns[:, owner_ids, column_group, :]
    pair_counts = counts[:, owner_ids, column_group]
    kk = jnp.arange(list_len, dtype=jnp.int32)
    panel_ids = jnp.arange(list_len, dtype=jnp.int32)
    hit = (pair_columns[None, :, :, :] == panel_ids[:, None, None, None]) & (
        kk[None, None, None, :] < pair_counts[None, :, :, None]
    )
    slot_valid = jnp.any(hit, axis=3)
    slot_k = jnp.sum(jnp.where(hit, kk[None, None, None, :], 0), axis=3)
    relation = jnp.arange(2, dtype=jnp.int32)
    slot_place = starts[None, None, :] + relation[None, :, None] * firsts[None, None, :] + slot_k
    slot_worker = jnp.transpose(slot_place % owners_count, (0, 2, 1)).reshape(-1)
    slot_valid = jnp.transpose(slot_valid, (0, 2, 1)).reshape(-1)
    blocks = jnp.take(incoming, slot_worker, axis=0)
    blocks = jnp.where(slot_valid[:, None, None], blocks, jnp.zeros((), blocks.dtype))
    per_panel = core_count * 2 * strip_rows
    blocks = blocks.reshape(list_len, per_panel, tile_cols)
    products = jnp.einsum(
        "jmt,jtf->jmf", blocks, panels.reshape(list_len, tile_cols, half), preferred_element_type=jnp.float32
    ).astype(jnp.bfloat16)
    sums = jnp.sum(products.astype(jnp.float32), axis=0).reshape(core_count, 2, strip_rows, half)
    my_weights = lax.dynamic_slice_in_dim(weights, my_core * half, half, axis=1)
    partial_value = None
    for q in range(2):
        lhs = sums[:, q].reshape(core_count * strip_rows, half)
        top = lhs.astype(jnp.bfloat16)
        rest = (lhs - top.astype(jnp.float32)).astype(jnp.bfloat16)
        part = jnp.dot(top, my_weights[q], preferred_element_type=jnp.float32)
        part = part + jnp.dot(rest, my_weights[q], preferred_element_type=jnp.float32)
        partial_value = part if partial_value is None else partial_value + part
    rep_count = lax.axis_size("rep")
    pieces = partial_value.reshape(core_count * rep_count, strip_rows // rep_count, feat_dim)
    pieces = lax.all_to_all(pieces, ("core", "rep"), split_axis=0, concat_axis=0, tiled=True)
    return jnp.sum(pieces, axis=0).astype(jnp.bfloat16)


def solution(mesh):
    dom_size, grp_size, rep_size = mesh.devices.shape
    split = jax.sharding.Mesh(
        mesh.devices.reshape(dom_size // 2, 2, grp_size, rep_size), ("z", "core", "grp", "rep")
    )
    return jax.shard_map(
        on_device,
        mesh=split,
        in_specs=(P(("rep", "grp"), None), P(("z", "core"), "rep", None, "grp", None), P(), P(), P()),
        out_specs=P(("z", "core", "grp", "rep"), None),
        check_vma=False,
    )
```

```python
import jax
import jax.numpy as jnp
from jax import lax
from jax.sharding import PartitionSpec as P


def on_device(features, tiles, columns, counts, weights):
    slot_count = tiles.shape[2]
    strip_rows = tiles.shape[3]
    tile_cols = tiles.shape[4]
    list_len = columns.shape[3]
    feat_dim = features.shape[1]
    chip_count = lax.axis_size("z")
    core_count = lax.axis_size("core")
    owners_count = chip_count * core_count
    my_core = lax.axis_index("core")
    me = lax.axis_index("z") * core_count + my_core
    column_group = lax.axis_index("rep")
    max_load = 2 * list_len

    swap = [(0, 1), (1, 0)]
    half = feat_dim // core_count
    mine = lax.dynamic_slice_in_dim(features, my_core * half, half, axis=1)
    grp_count = lax.axis_size("grp")
    spread = jnp.broadcast_to(mine[None], (grp_count,) + mine.shape)
    panels = lax.all_to_all(spread, "grp", split_axis=0, concat_axis=0, tiled=True)
    panels = panels.reshape(grp_count * mine.shape[0], half)

    first_counts = counts[0][:, column_group]
    group_loads = first_counts + counts[1][:, column_group]
    owner_starts = jnp.cumsum(group_loads) - group_loads

    strips = tiles.reshape(slot_count, strip_rows, tile_cols)
    chip_loads = group_loads.reshape(chip_count, core_count).sum(axis=1)
    chip_starts = owner_starts.reshape(chip_count, core_count)[:, 0]
    chip_slot = (chip_starts - me + owners_count - 1) // owners_count
    chip_slot = jnp.clip(chip_slot, 0, slot_count - 1)
    chip_place = me + chip_slot * owners_count
    chip_has = (chip_place >= chip_starts) & (chip_place < chip_starts + chip_loads)
    outgoing = jnp.where(chip_has[:, None, None], jnp.take(strips, chip_slot, axis=0), jnp.zeros((), strips.dtype))
    from_chips = lax.all_to_all(outgoing, "z", split_axis=0, concat_axis=0, tiled=True)
    from_sibling = lax.ppermute(from_chips, "core", swap)
    from_core0 = jnp.where(my_core == 0, from_chips, from_sibling)
    from_core1 = jnp.where(my_core == 0, from_sibling, from_chips)
    incoming = jnp.stack([from_core0, from_core1], axis=1).reshape(owners_count, strip_rows, tile_cols)

    chip_first = me - my_core
    owner_ids = chip_first + jnp.arange(core_count, dtype=jnp.int32)
    starts = owner_starts[owner_ids]
    firsts = first_counts[owner_ids]
    pair_columns = columns[:, owner_ids, column_group, :]
    pair_counts = counts[:, owner_ids, column_group]
    kk = jnp.arange(list_len, dtype=jnp.int32)
    panel_ids = jnp.arange(list_len, dtype=jnp.int32)
    hit = (pair_columns[None, :, :, :] == panel_ids[:, None, None, None]) & (
        kk[None, None, None, :] < pair_counts[None, :, :, None]
    )
    slot_valid = jnp.any(hit, axis=3)
    slot_k = jnp.sum(jnp.where(hit, kk[None, None, None, :], 0), axis=3)
    relation = jnp.arange(2, dtype=jnp.int32)
    slot_place = starts[None, None, :] + relation[None, :, None] * firsts[None, None, :] + slot_k
    slot_worker = jnp.transpose(slot_place % owners_count, (0, 2, 1)).reshape(-1)
    slot_valid = jnp.transpose(slot_valid, (0, 2, 1)).reshape(-1)
    blocks = jnp.take(incoming, slot_worker, axis=0)
    blocks = jnp.where(slot_valid[:, None, None], blocks, jnp.zeros((), blocks.dtype))
    per_panel = core_count * 2 * strip_rows
    blocks = blocks.reshape(list_len, per_panel, tile_cols)
    products = jnp.einsum(
        "jmt,jtf->jmf", blocks, panels.reshape(list_len, tile_cols, half), preferred_element_type=jnp.float32
    ).astype(jnp.bfloat16)
    sums = jnp.sum(products.astype(jnp.float32), axis=0).reshape(core_count, 2, strip_rows, half)
    my_weights = lax.dynamic_slice_in_dim(weights, my_core * half, half, axis=1)
    partial_value = None
    for q in range(2):
        lhs = sums[:, q].reshape(core_count * strip_rows, half)
        top = lhs.astype(jnp.bfloat16)
        rest = (lhs - top.astype(jnp.float32)).astype(jnp.bfloat16)
        part = jnp.dot(top, my_weights[q], preferred_element_type=jnp.float32)
        part = part + jnp.dot(rest, my_weights[q], preferred_element_type=jnp.float32)
        partial_value = part if partial_value is None else partial_value + part
    rep_count = lax.axis_size("rep")
    pieces = partial_value.reshape(core_count * rep_count, strip_rows // rep_count, feat_dim)
    pieces = lax.all_to_all(pieces, ("core", "rep"), split_axis=0, concat_axis=0, tiled=True)
    return jnp.sum(pieces, axis=0).astype(jnp.bfloat16)


def solution(mesh):
    dom_size, grp_size, rep_size = mesh.devices.shape
    split = jax.sharding.Mesh(
        mesh.devices.reshape(dom_size // 2, 2, grp_size, rep_size), ("z", "core", "grp", "rep")
    )
    return jax.shard_map(
        on_device,
        mesh=split,
        in_specs=(P(("rep", "grp"), None), P(("z", "core"), "rep", None, "grp", None), P(), P(), P()),
        out_specs=P(("z", "core", "grp", "rep"), None),
        check_vma=False,
    )
```

```python
import jax
import jax.numpy as jnp
from jax import lax
from jax.sharding import PartitionSpec as P


def on_device(features, tiles, columns, counts, weights):
    slot_count = tiles.shape[2]
    strip_rows = tiles.shape[3]
    tile_cols = tiles.shape[4]
    list_len = columns.shape[3]
    feat_dim = features.shape[1]
    chip_count = lax.axis_size("z")
    core_count = lax.axis_size("core")
    owners_count = chip_count * core_count
    my_core = lax.axis_index("core")
    me = lax.axis_index("z") * core_count + my_core
    column_group = lax.axis_index("rep")
    max_load = 2 * list_len

    swap = [(0, 1), (1, 0)]
    half = feat_dim // core_count
    mine = jnp.where(my_core == 0, features[:, :half], features[:, half:])
    panels = lax.all_gather(mine, "grp", axis=0, tiled=True)

    first_counts = counts[0][:, column_group]
    group_loads = first_counts + counts[1][:, column_group]
    owner_starts = jnp.cumsum(group_loads) - group_loads

    strips = tiles.reshape(slot_count, strip_rows, tile_cols)
    chip_loads = group_loads.reshape(chip_count, core_count).sum(axis=1)
    chip_starts = owner_starts.reshape(chip_count, core_count)[:, 0]
    chip_slot = (chip_starts - me + owners_count - 1) // owners_count
    chip_slot = jnp.clip(chip_slot, 0, slot_count - 1)
    chip_place = me + chip_slot * owners_count
    chip_has = (chip_place >= chip_starts) & (chip_place < chip_starts + chip_loads)
    outgoing = jnp.where(chip_has[:, None, None], jnp.take(strips, chip_slot, axis=0), jnp.zeros((), strips.dtype))
    from_chips = lax.all_to_all(outgoing, "z", split_axis=0, concat_axis=0, tiled=True)
    from_sibling = lax.ppermute(from_chips, "core", swap)
    from_core0 = jnp.where(my_core == 0, from_chips, from_sibling)
    from_core1 = jnp.where(my_core == 0, from_sibling, from_chips)
    incoming = jnp.stack([from_core0, from_core1], axis=1).reshape(owners_count, strip_rows, tile_cols)

    chip_first = me - my_core
    owner_ids = chip_first + jnp.arange(core_count, dtype=jnp.int32)
    starts = owner_starts[owner_ids]
    firsts = first_counts[owner_ids]
    pair_columns = columns[:, owner_ids, column_group, :]
    pair_counts = counts[:, owner_ids, column_group]
    kk = jnp.arange(list_len, dtype=jnp.int32)
    panel_ids = jnp.arange(list_len, dtype=jnp.int32)
    hit = (pair_columns[None, :, :, :] == panel_ids[:, None, None, None]) & (
        kk[None, None, None, :] < pair_counts[None, :, :, None]
    )
    slot_valid = jnp.any(hit, axis=3)
    slot_k = jnp.sum(jnp.where(hit, kk[None, None, None, :], 0), axis=3)
    relation = jnp.arange(2, dtype=jnp.int32)
    slot_place = starts[None, None, :] + relation[None, :, None] * firsts[None, None, :] + slot_k
    slot_worker = jnp.transpose(slot_place % owners_count, (0, 2, 1)).reshape(-1)
    slot_valid = jnp.transpose(slot_valid, (0, 2, 1)).reshape(-1)
    blocks = jnp.take(incoming, slot_worker, axis=0)
    blocks = jnp.where(slot_valid[:, None, None], blocks, jnp.zeros((), blocks.dtype))
    per_panel = core_count * 2 * strip_rows
    blocks = blocks.reshape(list_len, per_panel, tile_cols)
    products = jnp.einsum(
        "jmt,jtf->jmf", blocks, panels.reshape(list_len, tile_cols, half), preferred_element_type=jnp.float32
    ).astype(jnp.bfloat16)
    sums = jnp.sum(products.astype(jnp.float32), axis=0).reshape(core_count, 2, strip_rows, half)
    my_weights = lax.dynamic_slice_in_dim(weights, my_core * half, half, axis=1)
    partial_value = None
    for q in range(2):
        lhs = sums[:, q].reshape(core_count * strip_rows, half)
        top = lhs.astype(jnp.bfloat16)
        rest = (lhs - top.astype(jnp.float32)).astype(jnp.bfloat16)
        part = jnp.dot(top, my_weights[q], preferred_element_type=jnp.float32)
        part = part + jnp.dot(rest, my_weights[q], preferred_element_type=jnp.float32)
        partial_value = part if partial_value is None else partial_value + part
    rep_count = lax.axis_size("rep")
    pieces = partial_value.reshape(core_count * rep_count, strip_rows // rep_count, feat_dim)
    pieces = lax.all_to_all(pieces, ("core", "rep"), split_axis=0, concat_axis=0, tiled=True)
    return jnp.sum(pieces, axis=0).astype(jnp.bfloat16)


def solution(mesh):
    dom_size, grp_size, rep_size = mesh.devices.shape
    split = jax.sharding.Mesh(
        mesh.devices.reshape(dom_size // 2, 2, grp_size, rep_size), ("z", "core", "grp", "rep")
    )
    return jax.shard_map(
        on_device,
        mesh=split,
        in_specs=(P(("rep", "grp"), None), P(("z", "core"), "rep", None, "grp", None), P(), P(), P()),
        out_specs=P(("z", "core", "grp", "rep"), None),
        check_vma=False,
    )
```

```python
import jax
import jax.numpy as jnp
from jax import lax
from jax.sharding import PartitionSpec as P


def on_device(features, tiles, columns, counts, weights):
    slot_count = tiles.shape[2]
    strip_rows = tiles.shape[3]
    tile_cols = tiles.shape[4]
    list_len = columns.shape[3]
    feat_dim = features.shape[1]
    chip_count = lax.axis_size("z")
    core_count = lax.axis_size("core")
    owners_count = chip_count * core_count
    my_core = lax.axis_index("core")
    me = lax.axis_index("z") * core_count + my_core
    column_group = lax.axis_index("rep")
    max_load = 2 * list_len

    swap = [(0, 1), (1, 0)]
    half = feat_dim // core_count
    mine = jnp.where(my_core == 0, features[:, :half], features[:, half:])
    panels = lax.all_gather(mine, "grp", axis=0, tiled=True)

    first_counts = counts[0][:, column_group]
    group_loads = first_counts + counts[1][:, column_group]
    owner_starts = jnp.cumsum(group_loads) - group_loads

    strips = tiles.reshape(slot_count, strip_rows, tile_cols)
    chip_loads = group_loads.reshape(chip_count, core_count).sum(axis=1)
    chip_starts = owner_starts.reshape(chip_count, core_count)[:, 0]
    chip_slot = (chip_starts - me + owners_count - 1) // owners_count
    chip_slot = jnp.clip(chip_slot, 0, slot_count - 1)
    chip_place = me + chip_slot * owners_count
    chip_has = (chip_place >= chip_starts) & (chip_place < chip_starts + chip_loads)
    outgoing = jnp.where(chip_has[:, None, None], jnp.take(strips, chip_slot, axis=0), jnp.zeros((), strips.dtype))
    from_chips = lax.all_to_all(outgoing, "z", split_axis=0, concat_axis=0, tiled=True)
    from_sibling = lax.ppermute(from_chips, "core", swap)
    from_core0 = jnp.where(my_core == 0, from_chips, from_sibling)
    from_core1 = jnp.where(my_core == 0, from_sibling, from_chips)
    incoming = jnp.stack([from_core0, from_core1], axis=1).reshape(owners_count, strip_rows, tile_cols)

    chip_first = me - my_core
    owner_ids = chip_first + jnp.arange(core_count, dtype=jnp.int32)
    starts = owner_starts[owner_ids]
    firsts = first_counts[owner_ids]
    pair_columns = columns[:, owner_ids, column_group, :]
    pair_counts = counts[:, owner_ids, column_group]
    kk = jnp.arange(list_len, dtype=jnp.int32)
    panel_ids = jnp.arange(list_len, dtype=jnp.int32)
    hit = (pair_columns[None, :, :, :] == panel_ids[:, None, None, None]) & (
        kk[None, None, None, :] < pair_counts[None, :, :, None]
    )
    slot_valid = jnp.any(hit, axis=3)
    slot_k = jnp.sum(jnp.where(hit, kk[None, None, None, :], 0), axis=3)
    relation = jnp.arange(2, dtype=jnp.int32)
    slot_place = starts[None, None, :] + relation[None, :, None] * firsts[None, None, :] + slot_k
    slot_worker = jnp.transpose(slot_place % owners_count, (0, 2, 1)).reshape(-1)
    slot_valid = jnp.transpose(slot_valid, (0, 2, 1)).reshape(-1)
    blocks = jnp.take(incoming, slot_worker, axis=0)
    blocks = jnp.where(slot_valid[:, None, None], blocks, jnp.zeros((), blocks.dtype))
    per_panel = core_count * 2 * strip_rows
    blocks = blocks.reshape(list_len, per_panel, tile_cols)
    products = jnp.einsum(
        "jmt,jtf->jmf", blocks, panels.reshape(list_len, tile_cols, half), preferred_element_type=jnp.float32
    ).astype(jnp.bfloat16)
    sums = jnp.sum(products.astype(jnp.float32), axis=0).reshape(core_count, 2, strip_rows, half)
    my_weights = lax.dynamic_slice_in_dim(weights, my_core * half, half, axis=1)
    partial_value = None
    for q in range(2):
        lhs = sums[:, q].reshape(core_count * strip_rows, half)
        top = lhs.astype(jnp.bfloat16)
        rest = (lhs - top.astype(jnp.float32)).astype(jnp.bfloat16)
        part = jnp.dot(top, my_weights[q], preferred_element_type=jnp.float32)
        part = part + jnp.dot(rest, my_weights[q], preferred_element_type=jnp.float32)
        partial_value = part if partial_value is None else partial_value + part
    rep_count = lax.axis_size("rep")
    pieces = partial_value.reshape(core_count * rep_count, strip_rows // rep_count, feat_dim)
    pieces = lax.all_to_all(pieces.astype(jnp.bfloat16), ("core", "rep"), split_axis=0, concat_axis=0, tiled=True)
    return jnp.sum(pieces.astype(jnp.float32), axis=0).astype(jnp.bfloat16)


def solution(mesh):
    dom_size, grp_size, rep_size = mesh.devices.shape
    split = jax.sharding.Mesh(
        mesh.devices.reshape(dom_size // 2, 2, grp_size, rep_size), ("z", "core", "grp", "rep")
    )
    return jax.shard_map(
        on_device,
        mesh=split,
        in_specs=(P(("rep", "grp"), None), P(("z", "core"), "rep", None, "grp", None), P(), P(), P()),
        out_specs=P(("z", "core", "grp", "rep"), None),
        check_vma=False,
    )
```

```python
import jax
import jax.numpy as jnp
from jax import lax
from jax.sharding import PartitionSpec as P


def on_device(features, tiles, columns, counts, weights):
    slot_count = tiles.shape[2]
    strip_rows = tiles.shape[3]
    tile_cols = tiles.shape[4]
    list_len = columns.shape[3]
    feat_dim = features.shape[1]
    chip_count = lax.axis_size("z")
    core_count = lax.axis_size("core")
    owners_count = chip_count * core_count
    my_core = lax.axis_index("core")
    me = lax.axis_index("z") * core_count + my_core
    column_group = lax.axis_index("rep")
    max_load = 2 * list_len

    swap = [(0, 1), (1, 0)]
    half = feat_dim // core_count
    mine = jnp.where(my_core == 0, features[:, :half], features[:, half:])
    panels = lax.all_gather(mine, "grp", axis=0, tiled=True)

    first_counts = counts[0][:, column_group]
    group_loads = first_counts + counts[1][:, column_group]
    owner_starts = jnp.cumsum(group_loads) - group_loads

    strips = tiles.reshape(slot_count, strip_rows, tile_cols)
    chip_loads = group_loads.reshape(chip_count, core_count).sum(axis=1)
    chip_starts = owner_starts.reshape(chip_count, core_count)[:, 0]
    chip_slot = (chip_starts - me + owners_count - 1) // owners_count
    chip_slot = jnp.clip(chip_slot, 0, slot_count - 1)
    chip_place = me + chip_slot * owners_count
    chip_has = (chip_place >= chip_starts) & (chip_place < chip_starts + chip_loads)
    outgoing = jnp.where(chip_has[:, None, None], jnp.take(strips, chip_slot, axis=0), jnp.zeros((), strips.dtype))
    from_chips = lax.all_to_all(outgoing, "z", split_axis=0, concat_axis=0, tiled=True)
    from_sibling = lax.ppermute(from_chips, "core", swap)
    from_core0 = jnp.where(my_core == 0, from_chips, from_sibling)
    from_core1 = jnp.where(my_core == 0, from_sibling, from_chips)
    incoming = jnp.stack([from_core0, from_core1], axis=1).reshape(owners_count, strip_rows, tile_cols)

    chip_first = me - my_core
    owner_ids = chip_first + jnp.arange(core_count, dtype=jnp.int32)
    starts = owner_starts[owner_ids]
    firsts = first_counts[owner_ids]
    pair_columns = columns[:, owner_ids, column_group, :]
    pair_counts = counts[:, owner_ids, column_group]
    kk = jnp.arange(list_len, dtype=jnp.int32)
    panel_ids = jnp.arange(list_len, dtype=jnp.int32)
    hit = (pair_columns[None, :, :, :] == panel_ids[:, None, None, None]) & (
        kk[None, None, None, :] < pair_counts[None, :, :, None]
    )
    slot_valid = jnp.any(hit, axis=3)
    slot_k = jnp.sum(jnp.where(hit, kk[None, None, None, :], 0), axis=3)
    relation = jnp.arange(2, dtype=jnp.int32)
    slot_place = starts[None, None, :] + relation[None, :, None] * firsts[None, None, :] + slot_k
    slot_worker = jnp.transpose(slot_place % owners_count, (2, 1, 0)).reshape(-1)
    slot_valid = jnp.transpose(slot_valid, (2, 1, 0)).reshape(-1)
    blocks = jnp.take(incoming, slot_worker, axis=0)
    blocks = jnp.where(slot_valid[:, None, None], blocks, jnp.zeros((), blocks.dtype))
    blocks = blocks.reshape(core_count * 2, list_len, strip_rows, tile_cols)
    lhs_all = jnp.transpose(blocks, (0, 2, 1, 3)).reshape(core_count * 2 * strip_rows, list_len * tile_cols)
    sums = jnp.dot(lhs_all, panels, preferred_element_type=jnp.float32)
    sums = sums.reshape(core_count, 2, strip_rows, half)
    my_weights = lax.dynamic_slice_in_dim(weights, my_core * half, half, axis=1)
    partial_value = None
    for q in range(2):
        lhs = sums[:, q].reshape(core_count * strip_rows, half)
        top = lhs.astype(jnp.bfloat16)
        rest = (lhs - top.astype(jnp.float32)).astype(jnp.bfloat16)
        part = jnp.dot(top, my_weights[q], preferred_element_type=jnp.float32)
        part = part + jnp.dot(rest, my_weights[q], preferred_element_type=jnp.float32)
        partial_value = part if partial_value is None else partial_value + part
    rep_count = lax.axis_size("rep")
    pieces = partial_value.reshape(core_count * rep_count, strip_rows // rep_count, feat_dim)
    pieces = lax.all_to_all(pieces, ("core", "rep"), split_axis=0, concat_axis=0, tiled=True)
    return jnp.sum(pieces, axis=0).astype(jnp.bfloat16)


def solution(mesh):
    dom_size, grp_size, rep_size = mesh.devices.shape
    split = jax.sharding.Mesh(
        mesh.devices.reshape(dom_size // 2, 2, grp_size, rep_size), ("z", "core", "grp", "rep")
    )
    return jax.shard_map(
        on_device,
        mesh=split,
        in_specs=(P(("rep", "grp"), None), P(("z", "core"), "rep", None, "grp", None), P(), P(), P()),
        out_specs=P(("z", "core", "grp", "rep"), None),
        check_vma=False,
    )
```

```python
import jax
import jax.numpy as jnp
from jax import lax
from jax.sharding import PartitionSpec as P
from jax.experimental import pallas as pl
from jax.experimental.pallas import tpu as pltpu


def column_half(features, index, half):
    def body(idx_ref, x_hbm, o_hbm, sem):
        start = pl.multiple_of(idx_ref[0] * half, 128)
        copy = pltpu.make_async_copy(x_hbm.at[:, pl.ds(start, half)], o_hbm, sem)
        copy.start()
        copy.wait()

    return pl.pallas_call(
        body,
        out_shape=jax.ShapeDtypeStruct((features.shape[0], half), features.dtype),
        grid_spec=pltpu.PrefetchScalarGridSpec(
            num_scalar_prefetch=1,
            grid=(1,),
            in_specs=[pl.BlockSpec(memory_space=pl.ANY)],
            out_specs=pl.BlockSpec(memory_space=pl.ANY),
            scratch_shapes=[pltpu.SemaphoreType.DMA(())],
        ),
    )(index.reshape(1).astype(jnp.int32), features)


def on_device(features, tiles, columns, counts, weights):
    slot_count = tiles.shape[2]
    strip_rows = tiles.shape[3]
    tile_cols = tiles.shape[4]
    list_len = columns.shape[3]
    feat_dim = features.shape[1]
    chip_count = lax.axis_size("z")
    core_count = lax.axis_size("core")
    owners_count = chip_count * core_count
    my_core = lax.axis_index("core")
    me = lax.axis_index("z") * core_count + my_core
    column_group = lax.axis_index("rep")
    max_load = 2 * list_len

    swap = [(0, 1), (1, 0)]
    half = feat_dim // core_count
    mine = column_half(features, my_core, half)
    panels = lax.all_gather(mine, "grp", axis=0, tiled=True)

    first_counts = counts[0][:, column_group]
    group_loads = first_counts + counts[1][:, column_group]
    owner_starts = jnp.cumsum(group_loads) - group_loads

    strips = tiles.reshape(slot_count, strip_rows, tile_cols)
    chip_loads = group_loads.reshape(chip_count, core_count).sum(axis=1)
    chip_starts = owner_starts.reshape(chip_count, core_count)[:, 0]
    chip_slot = (chip_starts - me + owners_count - 1) // owners_count
    chip_slot = jnp.clip(chip_slot, 0, slot_count - 1)
    chip_place = me + chip_slot * owners_count
    chip_has = (chip_place >= chip_starts) & (chip_place < chip_starts + chip_loads)
    outgoing = jnp.where(chip_has[:, None, None], jnp.take(strips, chip_slot, axis=0), jnp.zeros((), strips.dtype))
    from_chips = lax.all_to_all(outgoing, "z", split_axis=0, concat_axis=0, tiled=True)
    from_sibling = lax.ppermute(from_chips, "core", swap)
    from_core0 = jnp.where(my_core == 0, from_chips, from_sibling)
    from_core1 = jnp.where(my_core == 0, from_sibling, from_chips)
    incoming = jnp.stack([from_core0, from_core1], axis=1).reshape(owners_count, strip_rows, tile_cols)

    chip_first = me - my_core
    owner_ids = chip_first + jnp.arange(core_count, dtype=jnp.int32)
    starts = owner_starts[owner_ids]
    firsts = first_counts[owner_ids]
    pair_columns = columns[:, owner_ids, column_group, :]
    pair_counts = counts[:, owner_ids, column_group]
    kk = jnp.arange(list_len, dtype=jnp.int32)
    panel_ids = jnp.arange(list_len, dtype=jnp.int32)
    hit = (pair_columns[None, :, :, :] == panel_ids[:, None, None, None]) & (
        kk[None, None, None, :] < pair_counts[None, :, :, None]
    )
    slot_valid = jnp.any(hit, axis=3)
    slot_k = jnp.sum(jnp.where(hit, kk[None, None, None, :], 0), axis=3)
    relation = jnp.arange(2, dtype=jnp.int32)
    slot_place = starts[None, None, :] + relation[None, :, None] * firsts[None, None, :] + slot_k
    slot_worker = jnp.transpose(slot_place % owners_count, (0, 2, 1)).reshape(-1)
    slot_valid = jnp.transpose(slot_valid, (0, 2, 1)).reshape(-1)
    blocks = jnp.take(incoming, slot_worker, axis=0)
    blocks = jnp.where(slot_valid[:, None, None], blocks, jnp.zeros((), blocks.dtype))
    per_panel = core_count * 2 * strip_rows
    blocks = blocks.reshape(list_len, per_panel, tile_cols)
    products = jnp.einsum(
        "jmt,jtf->jmf", blocks, panels.reshape(list_len, tile_cols, half), preferred_element_type=jnp.float32
    ).astype(jnp.bfloat16)
    sums = jnp.sum(products.astype(jnp.float32), axis=0).reshape(core_count, 2, strip_rows, half)
    my_weights = lax.dynamic_slice_in_dim(weights, my_core * half, half, axis=1)
    partial_value = None
    for q in range(2):
        lhs = sums[:, q].reshape(core_count * strip_rows, half)
        top = lhs.astype(jnp.bfloat16)
        rest = (lhs - top.astype(jnp.float32)).astype(jnp.bfloat16)
        part = jnp.dot(top, my_weights[q], preferred_element_type=jnp.float32)
        part = part + jnp.dot(rest, my_weights[q], preferred_element_type=jnp.float32)
        partial_value = part if partial_value is None else partial_value + part
    rep_count = lax.axis_size("rep")
    pieces = partial_value.reshape(core_count * rep_count, strip_rows // rep_count, feat_dim)
    pieces = lax.all_to_all(pieces, ("core", "rep"), split_axis=0, concat_axis=0, tiled=True)
    return jnp.sum(pieces, axis=0).astype(jnp.bfloat16)


def solution(mesh):
    dom_size, grp_size, rep_size = mesh.devices.shape
    split = jax.sharding.Mesh(
        mesh.devices.reshape(dom_size // 2, 2, grp_size, rep_size), ("z", "core", "grp", "rep")
    )
    return jax.shard_map(
        on_device,
        mesh=split,
        in_specs=(P(("rep", "grp"), None), P(("z", "core"), "rep", None, "grp", None), P(), P(), P()),
        out_specs=P(("z", "core", "grp", "rep"), None),
        check_vma=False,
    )
```

```python
import jax
import jax.numpy as jnp
from jax import lax
from jax.sharding import PartitionSpec as P


def on_device(features, tiles, columns, counts, weights):
    slot_count = tiles.shape[2]
    strip_rows = tiles.shape[3]
    tile_cols = tiles.shape[4]
    list_len = columns.shape[3]
    feat_dim = features.shape[1]
    chip_count = lax.axis_size("z")
    core_count = lax.axis_size("core")
    owners_count = chip_count * core_count
    my_core = lax.axis_index("core")
    me = lax.axis_index("z") * core_count + my_core
    column_group = lax.axis_index("rep")
    max_load = 2 * list_len

    swap = [(0, 1), (1, 0)]
    rows_half = features.shape[0] // core_count
    mine = jnp.where(my_core == 0, features[:rows_half], features[rows_half:])
    panels = lax.all_gather(mine, "grp", axis=0, tiled=True)

    first_counts = counts[0][:, column_group]
    group_loads = first_counts + counts[1][:, column_group]
    owner_starts = jnp.cumsum(group_loads) - group_loads

    strips = tiles.reshape(slot_count, strip_rows, tile_cols)
    chip_loads = group_loads.reshape(chip_count, core_count).sum(axis=1)
    chip_starts = owner_starts.reshape(chip_count, core_count)[:, 0]
    chip_slot = (chip_starts - me + owners_count - 1) // owners_count
    chip_slot = jnp.clip(chip_slot, 0, slot_count - 1)
    chip_place = me + chip_slot * owners_count
    chip_has = (chip_place >= chip_starts) & (chip_place < chip_starts + chip_loads)
    outgoing = jnp.where(chip_has[:, None, None], jnp.take(strips, chip_slot, axis=0), jnp.zeros((), strips.dtype))
    from_chips = lax.all_to_all(outgoing, "z", split_axis=0, concat_axis=0, tiled=True)
    from_sibling = lax.ppermute(from_chips, "core", swap)
    from_core0 = jnp.where(my_core == 0, from_chips, from_sibling)
    from_core1 = jnp.where(my_core == 0, from_sibling, from_chips)
    incoming = jnp.stack([from_core0, from_core1], axis=1).reshape(owners_count, strip_rows, tile_cols)

    chip_first = me - my_core
    owner_ids = chip_first + jnp.arange(core_count, dtype=jnp.int32)
    starts = owner_starts[owner_ids]
    firsts = first_counts[owner_ids]
    pair_columns = columns[:, owner_ids, column_group, :]
    pair_counts = counts[:, owner_ids, column_group]
    kk = jnp.arange(list_len, dtype=jnp.int32)
    panel_ids = jnp.arange(list_len, dtype=jnp.int32)
    hit = (pair_columns[None, :, :, :] == panel_ids[:, None, None, None]) & (
        kk[None, None, None, :] < pair_counts[None, :, :, None]
    )
    slot_valid = jnp.any(hit, axis=3)
    slot_k = jnp.sum(jnp.where(hit, kk[None, None, None, :], 0), axis=3)
    relation = jnp.arange(2, dtype=jnp.int32)
    slot_place = starts[None, None, :] + relation[None, :, None] * firsts[None, None, :] + slot_k
    slot_worker = jnp.transpose(slot_place % owners_count, (2, 1, 0)).reshape(-1)
    slot_valid = jnp.transpose(slot_valid, (2, 1, 0)).reshape(-1)
    blocks = jnp.take(incoming, slot_worker, axis=0)
    blocks = jnp.where(slot_valid[:, None, None], blocks, jnp.zeros((), blocks.dtype))
    blocks = blocks.reshape(core_count * 2, list_len, strip_rows, tile_cols)
    blocks = jnp.where(my_core == 0, blocks[..., :rows_half], blocks[..., rows_half:])
    lhs_all = jnp.transpose(blocks, (0, 2, 1, 3)).reshape(core_count * 2 * strip_rows, list_len * rows_half)
    sums = jnp.dot(lhs_all, panels, preferred_element_type=jnp.float32)
    sums = sums.reshape(core_count, 2, strip_rows, feat_dim)
    my_weights = weights
    partial_value = None
    for q in range(2):
        lhs = sums[:, q].reshape(core_count * strip_rows, feat_dim)
        top = lhs.astype(jnp.bfloat16)
        rest = (lhs - top.astype(jnp.float32)).astype(jnp.bfloat16)
        part = jnp.dot(top, my_weights[q], preferred_element_type=jnp.float32)
        part = part + jnp.dot(rest, my_weights[q], preferred_element_type=jnp.float32)
        partial_value = part if partial_value is None else partial_value + part
    rep_count = lax.axis_size("rep")
    pieces = partial_value.reshape(core_count * rep_count, strip_rows // rep_count, feat_dim)
    pieces = lax.all_to_all(pieces, ("core", "rep"), split_axis=0, concat_axis=0, tiled=True)
    return jnp.sum(pieces, axis=0).astype(jnp.bfloat16)


def solution(mesh):
    dom_size, grp_size, rep_size = mesh.devices.shape
    split = jax.sharding.Mesh(
        mesh.devices.reshape(dom_size // 2, 2, grp_size, rep_size), ("z", "core", "grp", "rep")
    )
    return jax.shard_map(
        on_device,
        mesh=split,
        in_specs=(P(("rep", "grp"), None), P(("z", "core"), "rep", None, "grp", None), P(), P(), P()),
        out_specs=P(("z", "core", "grp", "rep"), None),
        check_vma=False,
    )
```

```python
import jax
import jax.numpy as jnp
from jax import lax
from jax.sharding import PartitionSpec as P


def on_device(features, tiles, columns, counts, weights):
    slot_count = tiles.shape[2]
    strip_rows = tiles.shape[3]
    tile_cols = tiles.shape[4]
    list_len = columns.shape[3]
    feat_dim = features.shape[1]
    chip_count = lax.axis_size("z")
    core_count = lax.axis_size("core")
    owners_count = chip_count * core_count
    my_core = lax.axis_index("core")
    me = lax.axis_index("z") * core_count + my_core
    column_group = lax.axis_index("rep")
    max_load = 2 * list_len

    swap = [(0, 1), (1, 0)]
    half = feat_dim // core_count
    mine = jnp.where(my_core == 0, features[:, :half], features[:, half:])
    panels = lax.all_gather(mine, "grp", axis=0, tiled=True)

    first_counts = counts[0][:, column_group]
    group_loads = first_counts + counts[1][:, column_group]
    owner_starts = jnp.cumsum(group_loads) - group_loads

    strips = tiles.reshape(slot_count, strip_rows, tile_cols)
    chip_loads = group_loads.reshape(chip_count, core_count).sum(axis=1)
    chip_starts = owner_starts.reshape(chip_count, core_count)[:, 0]
    chip_slot = (chip_starts - me + owners_count - 1) // owners_count
    chip_slot = jnp.clip(chip_slot, 0, slot_count - 1)
    chip_place = me + chip_slot * owners_count
    chip_has = (chip_place >= chip_starts) & (chip_place < chip_starts + chip_loads)
    outgoing = jnp.where(chip_has[:, None, None], jnp.take(strips, chip_slot, axis=0), jnp.zeros((), strips.dtype))
    from_chips = lax.all_to_all(outgoing, "z", split_axis=0, concat_axis=0, tiled=True)
    from_sibling = lax.ppermute(from_chips, "core", swap)
    from_core0 = jnp.where(my_core == 0, from_chips, from_sibling)
    from_core1 = jnp.where(my_core == 0, from_sibling, from_chips)
    incoming = jnp.stack([from_core0, from_core1], axis=1).reshape(owners_count, strip_rows, tile_cols)

    chip_first = me - my_core
    owner_ids = chip_first + jnp.arange(core_count, dtype=jnp.int32)
    starts = owner_starts[owner_ids]
    firsts = first_counts[owner_ids]
    pair_columns = columns[:, owner_ids, column_group, :]
    pair_counts = counts[:, owner_ids, column_group]
    kk = jnp.arange(list_len, dtype=jnp.int32)
    panel_ids = jnp.arange(list_len, dtype=jnp.int32)
    hit = (pair_columns[None, :, :, :] == panel_ids[:, None, None, None]) & (
        kk[None, None, None, :] < pair_counts[None, :, :, None]
    )
    slot_valid = jnp.any(hit, axis=3)
    slot_k = jnp.sum(jnp.where(hit, kk[None, None, None, :], 0), axis=3)
    relation = jnp.arange(2, dtype=jnp.int32)
    slot_place = starts[None, None, :] + relation[None, :, None] * firsts[None, None, :] + slot_k
    slot_worker = jnp.transpose(slot_place % owners_count, (0, 2, 1)).reshape(-1)
    slot_valid = jnp.transpose(slot_valid, (0, 2, 1)).reshape(-1)
    blocks = jnp.take(incoming, slot_worker, axis=0)
    blocks = jnp.where(slot_valid[:, None, None], blocks, jnp.zeros((), blocks.dtype))
    per_panel = core_count * 2 * strip_rows
    blocks = blocks.reshape(list_len, per_panel, tile_cols)
    products = jnp.einsum(
        "jmt,jtf->jmf", blocks, panels.reshape(list_len, tile_cols, half), preferred_element_type=jnp.float32
    ).astype(jnp.bfloat16)
    sums = jnp.sum(products.astype(jnp.float32), axis=0).reshape(core_count, 2, strip_rows, half)
    my_weights = lax.dynamic_slice_in_dim(weights, my_core * half, half, axis=1)
    parts = []
    for q in range(2):
        lhs = sums[:, q].reshape(core_count * strip_rows, half)
        top = lhs.astype(jnp.bfloat16)
        parts += [top, (lhs - top.astype(jnp.float32)).astype(jnp.bfloat16)]
    stacked = jnp.concatenate([my_weights[0], my_weights[0], my_weights[1], my_weights[1]], axis=0)
    partial_value = jnp.dot(jnp.concatenate(parts, axis=1), stacked, preferred_element_type=jnp.float32)
    rep_count = lax.axis_size("rep")
    pieces = partial_value.reshape(core_count * rep_count, strip_rows // rep_count, feat_dim)
    pieces = lax.all_to_all(pieces, ("core", "rep"), split_axis=0, concat_axis=0, tiled=True)
    return jnp.sum(pieces, axis=0).astype(jnp.bfloat16)


def solution(mesh):
    dom_size, grp_size, rep_size = mesh.devices.shape
    split = jax.sharding.Mesh(
        mesh.devices.reshape(dom_size // 2, 2, grp_size, rep_size), ("z", "core", "grp", "rep")
    )
    return jax.shard_map(
        on_device,
        mesh=split,
        in_specs=(P(("rep", "grp"), None), P(("z", "core"), "rep", None, "grp", None), P(), P(), P()),
        out_specs=P(("z", "core", "grp", "rep"), None),
        check_vma=False,
    )
```

```python
import jax
import jax.numpy as jnp
from jax import lax
from jax.sharding import PartitionSpec as P


def on_device(features, tiles, columns, counts, weights):
    slot_count = tiles.shape[2]
    strip_rows = tiles.shape[3]
    tile_cols = tiles.shape[4]
    list_len = columns.shape[3]
    feat_dim = features.shape[1]
    chip_count = lax.axis_size("z")
    core_count = lax.axis_size("core")
    owners_count = chip_count * core_count
    my_core = lax.axis_index("core")
    me = lax.axis_index("z") * core_count + my_core
    column_group = lax.axis_index("rep")
    max_load = 2 * list_len

    swap = [(0, 1), (1, 0)]
    half = feat_dim // core_count
    mine = jnp.where(my_core == 0, features[:, :half], features[:, half:])
    panels = lax.all_gather(mine, "grp", axis=0, tiled=True)

    first_counts = counts[0][:, column_group]
    group_loads = first_counts + counts[1][:, column_group]
    owner_starts = jnp.cumsum(group_loads) - group_loads

    strips = tiles.reshape(slot_count, strip_rows, tile_cols)
    chip_loads = group_loads.reshape(chip_count, core_count).sum(axis=1)
    chip_starts = owner_starts.reshape(chip_count, core_count)[:, 0]
    chip_slot = (chip_starts - me + owners_count - 1) // owners_count
    chip_slot = jnp.clip(chip_slot, 0, slot_count - 1)
    chip_place = me + chip_slot * owners_count
    chip_has = (chip_place >= chip_starts) & (chip_place < chip_starts + chip_loads)
    outgoing = jnp.where(chip_has[:, None, None], jnp.take(strips, chip_slot, axis=0), jnp.zeros((), strips.dtype))
    from_chips = lax.all_to_all(outgoing, "z", split_axis=0, concat_axis=0, tiled=True)
    from_sibling = lax.ppermute(from_chips, "core", swap)
    from_core0 = jnp.where(my_core == 0, from_chips, from_sibling)
    from_core1 = jnp.where(my_core == 0, from_sibling, from_chips)
    incoming = jnp.stack([from_core0, from_core1], axis=1).reshape(owners_count, strip_rows, tile_cols)

    chip_first = me - my_core
    owner_ids = chip_first + jnp.arange(core_count, dtype=jnp.int32)
    starts = owner_starts[owner_ids]
    firsts = first_counts[owner_ids]
    pair_columns = columns[:, owner_ids, column_group, :]
    pair_counts = counts[:, owner_ids, column_group]
    kk = jnp.arange(list_len, dtype=jnp.int32)
    panel_ids = jnp.arange(list_len, dtype=jnp.int32)
    hit = (pair_columns[None, :, :, :] == panel_ids[:, None, None, None]) & (
        kk[None, None, None, :] < pair_counts[None, :, :, None]
    )
    slot_valid = jnp.any(hit, axis=3)
    slot_k = jnp.sum(jnp.where(hit, kk[None, None, None, :], 0), axis=3)
    relation = jnp.arange(2, dtype=jnp.int32)
    slot_place = starts[None, None, :] + relation[None, :, None] * firsts[None, None, :] + slot_k
    slot_worker = jnp.transpose(slot_place % owners_count, (0, 2, 1)).reshape(-1)
    slot_valid = jnp.transpose(slot_valid, (0, 2, 1)).reshape(-1)
    blocks = jnp.take(incoming, slot_worker, axis=0)
    blocks = jnp.where(slot_valid[:, None, None], blocks, jnp.zeros((), blocks.dtype))
    per_panel = core_count * 2 * strip_rows
    blocks = blocks.reshape(list_len, per_panel, tile_cols)
    products = jnp.einsum(
        "jmt,jtf->jmf", blocks, panels.reshape(list_len, tile_cols, half), preferred_element_type=jnp.float32
    ).astype(jnp.bfloat16)
    sums = jnp.sum(products.astype(jnp.float32), axis=0).reshape(core_count, 2, strip_rows, half)
    my_weights = lax.dynamic_slice_in_dim(weights, my_core * half, half, axis=1)
    parts = []
    for q in range(2):
        lhs = sums[:, q].reshape(core_count * strip_rows, half)
        top = lhs.astype(jnp.bfloat16)
        parts += [top, (lhs - top.astype(jnp.float32)).astype(jnp.bfloat16)]
    stacked = jnp.concatenate([my_weights[0], my_weights[0], my_weights[1], my_weights[1]], axis=0)
    partial_value = jnp.dot(jnp.concatenate(parts, axis=1), stacked, preferred_element_type=jnp.float32)
    rep_count = lax.axis_size("rep")
    pieces = partial_value.reshape(core_count * rep_count, strip_rows // rep_count, feat_dim)
    pieces = lax.all_to_all(pieces.astype(jnp.bfloat16), ("core", "rep"), split_axis=0, concat_axis=0, tiled=True)
    return jnp.sum(pieces.astype(jnp.float32), axis=0).astype(jnp.bfloat16)


def solution(mesh):
    dom_size, grp_size, rep_size = mesh.devices.shape
    split = jax.sharding.Mesh(
        mesh.devices.reshape(dom_size // 2, 2, grp_size, rep_size), ("z", "core", "grp", "rep")
    )
    return jax.shard_map(
        on_device,
        mesh=split,
        in_specs=(P(("rep", "grp"), None), P(("z", "core"), "rep", None, "grp", None), P(), P(), P()),
        out_specs=P(("z", "core", "grp", "rep"), None),
        check_vma=False,
    )
```
